1024 devices in a mesh: group: 64 (over y, z_hi, core), blk: 16 (over x, z_lo).
Axes of the slice: x: 4, y: 8, z: 16 (z_hi: 4, z_lo: 4; z = z_hi * 4 + z_lo), core: 2. Of those that a mesh axis runs over, the one named last changes fastest.
Arguments:
- informal: bfloat16 [131072, 1024], P(('group', 'blk')), may hold values from -6 to 6
- formal: bfloat16 [131072, 1024], P(('group', 'blk')), may hold values from -6 to 6
- labels: int32 [131072], P(('group', 'blk')), may hold values from 0 to 2047
- temp: float32 [], replicated, may hold values from 2 to 4
- bias: float32 [], replicated, may hold values from -3 to -1
Outputs:
- loss: float32 [131072], P(('group', 'blk'))
- grad_informal: float32 [131072, 1024], P(('group', 'blk'))
- grad_formal: float32 [131072, 1024], P(('group', 'blk'))
- grad_temp: float32 [], replicated
- grad_bias: float32 [], replicated
The draws below stay inside these ranges and needn't reach their ends.
All inputs are finite; a program needn't handle non-finite values.
Results may differ from the reference program's by a relative error of at most 0.0025.
Values may be sent and summed in bfloat16 or wider, within the bound.
No kernel may reach another device: no remote copies, remote signals or barrier semaphores. Data moves between devices by JAX's collectives and lax.ppermute only.
A program may use at most 32 MiB of HBM per device.

```python
import math
import jax
import jax.numpy as jnp
from jax import lax

D = 1024
SET = 2048
BATCH = 131072


def plant(array, own_key, least, largest):
    dims = array.shape
    index_at = [jax.random.randint(jax.random.fold_in(own_key, axis), (), 0, dims[axis]) for axis in range(len(dims))]
    array = array.at[tuple(index_at)].set(least)
    longest = dims.index(max(dims))
    index_at[longest] = (index_at[longest] + 1) % dims[longest]
    return array.at[tuple(index_at)].set(largest)


def level_of(stream_key, extent, split, least, top_value):
    def one(axis_at, blocks):
        draws = jax.random.uniform(jax.random.fold_in(jax.random.fold_in(stream_key, 6), axis_at), (blocks,), jnp.float32, least / len(split), top_value / len(split))
        return jnp.repeat(jnp.exp(draws), extent[axis_at] // blocks).reshape((-1,) + (1,) * (len(extent) - axis_at - 1))

    gain = one(*split[0])
    for cut in split[1:]:
        gain = gain * one(*cut)
    return gain


def normal_values(key, shape, scale, bound, shards=(), kind=jnp.bfloat16):
    values = scale * jax.random.normal(key, shape, jnp.float32)
    if shards:
        values = values * level_of(key, shape, shards, -0.22, 0.18)
    return jnp.clip(values, -bound, bound).astype(kind)


def setup_inputs(seed: int = 0) -> dict:
    splits = jax.random.split(jax.random.key(seed), 6)
    informal = normal_values(splits[0], (BATCH, D), 1.0, 6.0, ((0, 1024),))
    formal = normal_values(splits[1], (BATCH, D), 1.0, 6.0, ((0, 1024),))
    labels = plant(jax.random.randint(splits[2], (BATCH,), 0, SET), jax.random.fold_in(splits[2], 1), 0, SET - 1).astype(jnp.int32)
    temp = jnp.clip(jax.random.uniform(splits[3], (), jnp.float32, 2.0, 4.0), 2.0, 4.0)
    bias = jnp.clip(jax.random.uniform(splits[4], (), jnp.float32, -3.0, -1.0), -3.0, -1.0)
    return dict(informal=informal, formal=formal, labels=labels, temp=temp, bias=bias)


def one_set(args, temp, bias):
    informal, formal, labels = args
    raw = jnp.dot(informal, formal.T, preferred_element_type=jnp.float32) / math.sqrt(D)
    logits = temp * raw + bias
    sign = jnp.where(labels[:, None] == labels[None, :], 1.0, -1.0).astype(jnp.float32)
    loss = lax.optimization_barrier(jnp.sum(jax.nn.softplus(-sign * logits), axis=1)) / SET
    slope = -sign * jax.nn.sigmoid(-sign * logits)
    weights = slope.astype(jnp.bfloat16)
    scale = temp / math.sqrt(D)
    grad_informal = scale * jnp.dot(weights, formal, preferred_element_type=jnp.float32)
    grad_formal = scale * jnp.dot(weights.T, informal, preferred_element_type=jnp.float32)
    return (loss, grad_informal, grad_formal, jnp.sum(slope * raw), jnp.sum(slope))

def reference(informal, formal, labels, temp, bias):
    nsets = BATCH // SET
    parts = (informal.reshape(nsets, SET, D), formal.reshape(nsets, SET, D), labels.reshape(nsets, SET))
    loss, grad_informal, grad_formal, temp_sums, bias_sums = lax.map(lambda a: one_set(a, temp, bias), parts)
    total = jnp.float32(BATCH) * jnp.float32(SET)
    return (loss.reshape(BATCH), grad_informal.reshape(BATCH, D), grad_formal.reshape(BATCH, D), jnp.sum(temp_sums) / total, jnp.sum(bias_sums) / total)
```

```python
import math

import jax
import jax.numpy as jnp
from jax import lax
from jax.sharding import Mesh
from jax.sharding import PartitionSpec as P


def shifted(value, axis, by):
    count = lax.axis_size(axis)
    return lax.ppermute(value, axis, [(i, (i + by) % count) for i in range(count)])


def gather_by_shift(value, axis):
    count = lax.axis_size(axis)
    return jnp.concatenate([value] + [shifted(value, axis, k) for k in range(1, count)], axis=0)


def reduce_by_shift(parts, axis):
    count = lax.axis_size(axis)
    total = parts[0]
    for k in range(1, count):
        total = total + shifted(parts[k], axis, -k)
    return total


def total_sums(sums, axes):
    for axis in axes:
        count = lax.axis_size(axis)
        step = 1
        while step < count:
            if step * 4 <= count:
                got = [lax.ppermute(sums, axis, [(i, i ^ (a * step)) for i in range(count)]) for a in (1, 2, 3)]
                sums = (sums + got[0]) + (got[1] + got[2])
                step *= 4
            else:
                sums = sums + lax.ppermute(sums, axis, [(i, i ^ step) for i in range(count)])
                step *= 2
    return sums


def on_device(informal, formal, labels, temp, bias):
    rows, width = informal.shape
    ngroup = lax.axis_size("group")
    nrow = lax.axis_size("bz")
    ncol = lax.axis_size("bx")
    root = math.sqrt(width)
    scale = temp / root
    row_informal = gather_by_shift(informal, "bz")
    row_labels = gather_by_shift(labels, "bz")
    col_formal = gather_by_shift(formal, "bx")
    col_labels = gather_by_shift(labels, "bx")
    raw = lax.dot_general(row_informal, col_formal, (((1,), (1,)), ((), ())), preferred_element_type=jnp.float32) / root
    logits = temp * raw + bias
    sign = jnp.where(row_labels[:, None] == col_labels[None, :], 1.0, -1.0).astype(jnp.float32)
    loss_part = jnp.sum(jax.nn.softplus(-sign * logits), axis=1)
    slope = -sign * jax.nn.sigmoid(-sign * logits)
    weights = slope.astype(jnp.bfloat16)
    grad_x_part = jnp.dot(weights, col_formal, preferred_element_type=jnp.float32)
    grad_y_part = lax.dot_general(weights, row_informal, (((0,), (0,)), ((), ())), preferred_element_type=jnp.float32)
    sums = total_sums(jnp.stack([jnp.sum(slope * raw), jnp.sum(slope)]), ("group", "bx", "bz"))
    loss_sum = reduce_by_shift(loss_part.reshape(nrow, rows), "bz")
    grad_x = scale * reduce_by_shift(grad_x_part.reshape(nrow, rows, width), "bz")
    grad_y = scale * reduce_by_shift(grad_y_part.reshape(ncol, rows, width), "bx")
    set_size = rows * nrow * ncol
    total = jnp.float32(set_size * ngroup) * jnp.float32(set_size)
    loss = loss_sum / set_size
    return (loss, grad_x, grad_y, sums[0] / total, sums[1] / total)


def split_blk(mesh):
    blk = mesh.devices[0]
    nx = len({d.coords[0] for d in blk})
    grid = mesh.devices.reshape(mesh.shape["group"], nx, blk.size // nx)
    return Mesh(grid, ("group", "bx", "bz"))


def solution(mesh):
    fine = split_blk(mesh)
    rowspec = ("group", "bx", "bz")
    in_specs = (P(rowspec, None), P(rowspec, None), P(rowspec), P(), P())
    out_specs = (P(rowspec), P(rowspec, None), P(rowspec, None), P(), P())
    return jax.shard_map(on_device, mesh=fine, in_specs=in_specs, out_specs=out_specs, check_vma=False)
```

```python
import math

import jax
import jax.numpy as jnp
from jax import lax
from jax.sharding import Mesh
from jax.sharding import PartitionSpec as P


def shifted(value, axis, by):
    count = lax.axis_size(axis)
    return lax.ppermute(value, axis, [(i, (i + by) % count) for i in range(count)])


def gather_by_shift(value, axis):
    count = lax.axis_size(axis)
    return jnp.concatenate([value] + [shifted(value, axis, k) for k in range(1, count)], axis=0)


def reduce_by_shift(parts, axis):
    count = lax.axis_size(axis)
    total = parts[0]
    for k in range(1, count):
        total = total + shifted(parts[k], axis, -k)
    return total


def total_sums(sums, axes):
    for axis in axes:
        count = lax.axis_size(axis)
        step = 1
        while step < count:
            sums = sums + lax.ppermute(sums, axis, [(i, i ^ step) for i in range(count)])
            step *= 2
    return sums


def device_terms(informal, formal, labels, temp, bias):
    rows, width = informal.shape
    ngroup = lax.axis_size("group")
    nrow = lax.axis_size("bz")
    ncol = lax.axis_size("bx")
    root = math.sqrt(width)
    scale = temp / root
    row_informal = gather_by_shift(informal, "bz")
    row_labels = gather_by_shift(labels, "bz")
    col_formal = gather_by_shift(formal, "bx")
    col_labels = gather_by_shift(labels, "bx")
    raw = lax.dot_general(row_informal, col_formal, (((1,), (1,)), ((), ())), preferred_element_type=jnp.float32) / root
    logits = temp * raw + bias
    sign = jnp.where(row_labels[:, None] == col_labels[None, :], 1.0, -1.0).astype(jnp.float32)
    loss_part = jnp.sum(jax.nn.softplus(-sign * logits), axis=1)
    slope = -sign * jax.nn.sigmoid(-sign * logits)
    weights = slope.astype(jnp.bfloat16)
    grad_x_part = jnp.dot(weights, col_formal, preferred_element_type=jnp.float32)
    grad_y_part = lax.dot_general(weights, row_informal, (((0,), (0,)), ((), ())), preferred_element_type=jnp.float32)
    loss_sum = reduce_by_shift(loss_part.reshape(nrow, rows), "bz")
    grad_x = scale * reduce_by_shift(grad_x_part.reshape(nrow, rows, width), "bz")
    grad_y = scale * reduce_by_shift(grad_y_part.reshape(ncol, rows, width), "bx")
    sums = total_sums(jnp.stack([jnp.sum(slope * raw), jnp.sum(slope)]), ("group", "bx", "bz"))
    set_size = rows * nrow * ncol
    total = jnp.float32(set_size * ngroup) * jnp.float32(set_size)
    loss = loss_sum / set_size
    return (loss, grad_x, grad_y, sums[0] / total, sums[1] / total)


def split_blk(mesh):
    blk = mesh.devices[0]
    nx = len({d.coords[0] for d in blk})
    grid = mesh.devices.reshape(mesh.shape["group"], nx, blk.size // nx)
    return Mesh(grid, ("group", "bx", "bz"))


def solution(mesh):
    fine = split_blk(mesh)
    rowspec = ("group", "bx", "bz")
    in_specs = (P(rowspec, None), P(rowspec, None), P(rowspec), P(), P())
    out_specs = (P(rowspec), P(rowspec, None), P(rowspec, None), P(), P())
    return jax.shard_map(device_terms, mesh=fine, in_specs=in_specs, out_specs=out_specs, check_vma=False)
```

```python
import math

import jax
import jax.numpy as jnp
from jax import lax
from jax.sharding import Mesh
from jax.sharding import PartitionSpec as P


def shifted(value, axis, by):
    count = lax.axis_size(axis)
    return lax.ppermute(value, axis, [(i, (i + by) % count) for i in range(count)])


def gather_by_shift(value, axis):
    count = lax.axis_size(axis)
    return jnp.concatenate([value] + [shifted(value, axis, k) for k in range(1, count)], axis=0)


def reduce_by_shift(parts, axis):
    count = lax.axis_size(axis)
    total = parts[0]
    for k in range(1, count):
        total = total + shifted(parts[k], axis, -k)
    return total


def with_labels(block, labels):
    rows, width = block.shape
    assert rows <= width
    shifts = 8 * jnp.arange(4, dtype=jnp.int32)
    digits = (labels[None, :] >> shifts[:, None]) & 255
    tail = jnp.zeros((16, width), block.dtype).at[:4, :rows].set(digits.astype(block.dtype))
    return jnp.concatenate([block, tail], axis=0)


def split_labels(gathered, rows):
    width = gathered.shape[1]
    pieces = gathered.reshape(-1, rows + 16, width)
    data = pieces[:, :rows].reshape(-1, width)
    digits = pieces[:, rows : rows + 4, :rows].astype(jnp.int32)
    labels = digits[:, 0] | (digits[:, 1] << 8) | (digits[:, 2] << 16) | (digits[:, 3] << 24)
    return data, labels.reshape(-1)


def with_loss(grad_part, loss_part):
    count, rows, width = grad_part.shape
    tail = jnp.zeros((count, 8, width), grad_part.dtype).at[:, 0, :rows].set(loss_part)
    return jnp.concatenate([grad_part, tail], axis=1)


def total_sums(sums, axes):
    for axis in axes:
        count = lax.axis_size(axis)
        step = 1
        while step < count:
            sums = sums + lax.ppermute(sums, axis, [(i, i ^ step) for i in range(count)])
            step *= 2
    return sums


def device_terms(informal, formal, labels, temp, bias):
    rows, width = informal.shape
    ngroup = lax.axis_size("group")
    nrow = lax.axis_size("bz")
    ncol = lax.axis_size("bx")
    root = math.sqrt(width)
    scale = temp / root
    row_informal, row_labels = split_labels(gather_by_shift(with_labels(informal, labels), "bz"), rows)
    col_formal, col_labels = split_labels(gather_by_shift(with_labels(formal, labels), "bx"), rows)
    raw = lax.dot_general(row_informal, col_formal, (((1,), (1,)), ((), ())), preferred_element_type=jnp.float32) / root
    logits = temp * raw + bias
    sign = jnp.where(row_labels[:, None] == col_labels[None, :], 1.0, -1.0).astype(jnp.float32)
    loss_part = jnp.sum(jax.nn.softplus(-sign * logits), axis=1)
    slope = -sign * jax.nn.sigmoid(-sign * logits)
    weights = slope.astype(jnp.bfloat16)
    grad_x_part = jnp.dot(weights, col_formal, preferred_element_type=jnp.float32)
    grad_y_part = lax.dot_general(weights, row_informal, (((0,), (0,)), ((), ())), preferred_element_type=jnp.float32)
    packed = reduce_by_shift(with_loss(grad_x_part.reshape(nrow, rows, width), loss_part.reshape(nrow, rows)), "bz")
    loss_sum = packed[rows, :rows]
    grad_x = scale * packed[:rows]
    grad_y = scale * reduce_by_shift(grad_y_part.reshape(ncol, rows, width), "bx")
    sums = total_sums(jnp.stack([jnp.sum(slope * raw), jnp.sum(slope)]), ("group", "bx", "bz"))
    set_size = rows * nrow * ncol
    total = jnp.float32(set_size * ngroup) * jnp.float32(set_size)
    loss = loss_sum / set_size
    return (loss, grad_x, grad_y, sums[0] / total, sums[1] / total)


def split_blk(mesh):
    blk = mesh.devices[0]
    nx = len({d.coords[0] for d in blk})
    grid = mesh.devices.reshape(mesh.shape["group"], nx, blk.size // nx)
    return Mesh(grid, ("group", "bx", "bz"))


def solution(mesh):
    fine = split_blk(mesh)
    rowspec = ("group", "bx", "bz")
    in_specs = (P(rowspec, None), P(rowspec, None), P(rowspec), P(), P())
    out_specs = (P(rowspec), P(rowspec, None), P(rowspec, None), P(), P())
    return jax.shard_map(device_terms, mesh=fine, in_specs=in_specs, out_specs=out_specs, check_vma=False)
```

```python
import math

import jax
import jax.numpy as jnp
from jax import lax
from jax.sharding import Mesh
from jax.sharding import PartitionSpec as P


def shifted(value, axis, by):
    count = lax.axis_size(axis)
    return lax.ppermute(value, axis, [(i, (i + by) % count) for i in range(count)])


def gather_by_shift(value, axis):
    count = lax.axis_size(axis)
    return jnp.concatenate([value] + [shifted(value, axis, k) for k in range(1, count)], axis=0)


def reduce_by_shift(parts, axis):
    count = lax.axis_size(axis)
    total = parts[0]
    for k in range(1, count):
        total = total + shifted(parts[k], axis, -k)
    return total


def with_labels(block, labels):
    rows, width = block.shape
    assert rows <= width
    shifts = 8 * jnp.arange(4, dtype=jnp.int32)
    digits = (labels[None, :] >> shifts[:, None]) & 255
    tail = jnp.zeros((16, width), block.dtype).at[:4, :rows].set(digits.astype(block.dtype))
    return jnp.concatenate([block, tail], axis=0)


def split_labels(gathered, rows):
    width = gathered.shape[1]
    pieces = gathered.reshape(-1, rows + 16, width)
    data = pieces[:, :rows].reshape(-1, width)
    digits = pieces[:, rows : rows + 4, :rows].astype(jnp.int32)
    labels = digits[:, 0] | (digits[:, 1] << 8) | (digits[:, 2] << 16) | (digits[:, 3] << 24)
    return data, labels.reshape(-1)


def with_loss(grad_part, loss_part):
    count, rows, width = grad_part.shape
    tail = jnp.zeros((count, 8, width), grad_part.dtype).at[:, 0, :rows].set(loss_part)
    return jnp.concatenate([grad_part, tail], axis=1)


def total_sums(sums, axes):
    for axis in axes:
        count = lax.axis_size(axis)
        step = 1
        while step < count:
            if step * 4 <= count:
                got = [lax.ppermute(sums, axis, [(i, i ^ (a * step)) for i in range(count)]) for a in (1, 2, 3)]
                sums = (sums + got[0]) + (got[1] + got[2])
                step *= 4
            else:
                sums = sums + lax.ppermute(sums, axis, [(i, i ^ step) for i in range(count)])
                step *= 2
    return sums


def device_terms(informal, formal, labels, temp, bias):
    rows, width = informal.shape
    ngroup = lax.axis_size("group")
    nrow = lax.axis_size("bz")
    ncol = lax.axis_size("bx")
    root = math.sqrt(width)
    scale = temp / root
    row_informal, row_labels = split_labels(gather_by_shift(with_labels(informal, labels), "bz"), rows)
    col_formal, col_labels = split_labels(gather_by_shift(with_labels(formal, labels), "bx"), rows)
    raw = lax.dot_general(row_informal, col_formal, (((1,), (1,)), ((), ())), preferred_element_type=jnp.float32) / root
    logits = temp * raw + bias
    sign = jnp.where(row_labels[:, None] == col_labels[None, :], 1.0, -1.0).astype(jnp.float32)
    loss_part = jnp.sum(jax.nn.softplus(-sign * logits), axis=1)
    slope = -sign * jax.nn.sigmoid(-sign * logits)
    weights = slope.astype(jnp.bfloat16)
    grad_x_part = jnp.dot(weights, col_formal, preferred_element_type=jnp.float32)
    grad_y_part = lax.dot_general(weights, row_informal, (((0,), (0,)), ((), ())), preferred_element_type=jnp.float32)
    packed = reduce_by_shift(with_loss(grad_x_part.reshape(nrow, rows, width), loss_part.reshape(nrow, rows)), "bz")
    loss_sum = packed[rows, :rows]
    grad_x = scale * packed[:rows]
    grad_y = scale * reduce_by_shift(grad_y_part.reshape(ncol, rows, width), "bx")
    sums = total_sums(jnp.stack([jnp.sum(slope * raw), jnp.sum(slope)]), ("group", "bx", "bz"))
    set_size = rows * nrow * ncol
    total = jnp.float32(set_size * ngroup) * jnp.float32(set_size)
    loss = loss_sum / set_size
    return (loss, grad_x, grad_y, sums[0] / total, sums[1] / total)


def split_blk(mesh):
    blk = mesh.devices[0]
    nx = len({d.coords[0] for d in blk})
    grid = mesh.devices.reshape(mesh.shape["group"], nx, blk.size // nx)
    return Mesh(grid, ("group", "bx", "bz"))


def solution(mesh):
    fine = split_blk(mesh)
    rowspec = ("group", "bx", "bz")
    in_specs = (P(rowspec, None), P(rowspec, None), P(rowspec), P(), P())
    out_specs = (P(rowspec), P(rowspec, None), P(rowspec, None), P(), P())
    return jax.shard_map(device_terms, mesh=fine, in_specs=in_specs, out_specs=out_specs, check_vma=False)
```

```python
import math

import jax
import jax.numpy as jnp
from jax import lax
from jax.sharding import Mesh
from jax.sharding import PartitionSpec as P


def gather_all(value, axis):
    count = lax.axis_size(axis)
    return lax.all_to_all(jnp.tile(value, (count, 1)), axis, 0, 0, tiled=True)


def reduce_all(parts, axis):
    count = lax.axis_size(axis)
    got = lax.all_to_all(parts, axis, 0, 0, tiled=True)
    total = got[0]
    for k in range(1, count):
        total = total + got[k]
    return total


def with_labels(block, labels):
    rows, width = block.shape
    assert rows <= width
    shifts = 8 * jnp.arange(4, dtype=jnp.int32)
    digits = (labels[None, :] >> shifts[:, None]) & 255
    tail = jnp.zeros((16, width), block.dtype).at[:4, :rows].set(digits.astype(block.dtype))
    return jnp.concatenate([block, tail], axis=0)


def split_labels(gathered, rows):
    width = gathered.shape[1]
    pieces = gathered.reshape(-1, rows + 16, width)
    data = pieces[:, :rows].reshape(-1, width)
    digits = pieces[:, rows : rows + 4, :rows].astype(jnp.int32)
    labels = digits[:, 0] | (digits[:, 1] << 8) | (digits[:, 2] << 16) | (digits[:, 3] << 24)
    return data, labels.reshape(-1)


def with_loss(grad_part, loss_part):
    count, rows, width = grad_part.shape
    tail = jnp.zeros((count, 8, width), grad_part.dtype).at[:, 0, :rows].set(loss_part)
    return jnp.concatenate([grad_part, tail], axis=1)


def total_sums(sums, axes):
    for axis in axes:
        count = lax.axis_size(axis)
        step = 1
        while step < count:
            sums = sums + lax.ppermute(sums, axis, [(i, i ^ step) for i in range(count)])
            step *= 2
    return sums


def device_terms(informal, formal, labels, temp, bias):
    rows, width = informal.shape
    ngroup = lax.axis_size("group")
    nrow = lax.axis_size("bz")
    ncol = lax.axis_size("bx")
    root = math.sqrt(width)
    scale = temp / root
    row_informal, row_labels = split_labels(gather_all(with_labels(informal, labels), "bz"), rows)
    col_formal, col_labels = split_labels(gather_all(with_labels(formal, labels), "bx"), rows)
    raw = lax.dot_general(row_informal, col_formal, (((1,), (1,)), ((), ())), preferred_element_type=jnp.float32) / root
    logits = temp * raw + bias
    sign = jnp.where(row_labels[:, None] == col_labels[None, :], 1.0, -1.0).astype(jnp.float32)
    loss_part = jnp.sum(jax.nn.softplus(-sign * logits), axis=1)
    slope = -sign * jax.nn.sigmoid(-sign * logits)
    weights = slope.astype(jnp.bfloat16)
    grad_x_part = jnp.dot(weights, col_formal, preferred_element_type=jnp.float32)
    grad_y_part = lax.dot_general(weights, row_informal, (((0,), (0,)), ((), ())), preferred_element_type=jnp.float32)
    packed = reduce_all(with_loss(grad_x_part.reshape(nrow, rows, width), loss_part.reshape(nrow, rows)), "bz")
    loss_sum = packed[rows, :rows]
    grad_x = scale * packed[:rows]
    grad_y = scale * reduce_all(grad_y_part.reshape(ncol, rows, width), "bx")
    sums = total_sums(jnp.stack([jnp.sum(slope * raw), jnp.sum(slope)]), ("group", "bx", "bz"))
    set_size = rows * nrow * ncol
    total = jnp.float32(set_size * ngroup) * jnp.float32(set_size)
    loss = loss_sum / set_size
    return (loss, grad_x, grad_y, sums[0] / total, sums[1] / total)


def split_blk(mesh):
    blk = mesh.devices[0]
    nx = len({d.coords[0] for d in blk})
    grid = mesh.devices.reshape(mesh.shape["group"], nx, blk.size // nx)
    return Mesh(grid, ("group", "bx", "bz"))


def solution(mesh):
    fine = split_blk(mesh)
    rowspec = ("group", "bx", "bz")
    in_specs = (P(rowspec, None), P(rowspec, None), P(rowspec), P(), P())
    out_specs = (P(rowspec), P(rowspec, None), P(rowspec, None), P(), P())
    return jax.shard_map(device_terms, mesh=fine, in_specs=in_specs, out_specs=out_specs, check_vma=False)
```

```python
import math

import jax
import jax.numpy as jnp
from jax import lax
from jax.sharding import Mesh
from jax.sharding import PartitionSpec as P


def shifted(value, axis, by):
    count = lax.axis_size(axis)
    return lax.ppermute(value, axis, [(i, (i + by) % count) for i in range(count)])


def gather_by_shift(value, axis):
    count = lax.axis_size(axis)
    return jnp.concatenate([value] + [shifted(value, axis, k) for k in range(1, count)], axis=0)


def reduce_by_shift(parts, axis):
    count = lax.axis_size(axis)
    total = parts[0]
    for k in range(1, count):
        total = total + shifted(parts[k], axis, -k)
    return total


def with_labels(block, labels):
    rows, width = block.shape
    assert rows <= width
    shifts = 8 * jnp.arange(4, dtype=jnp.int32)
    digits = (labels[None, :] >> shifts[:, None]) & 255
    tail = jnp.zeros((16, width), block.dtype).at[:4, :rows].set(digits.astype(block.dtype))
    return jnp.concatenate([block, tail], axis=0)


def split_labels(gathered, rows):
    width = gathered.shape[1]
    pieces = gathered.reshape(-1, rows + 16, width)
    data = pieces[:, :rows].reshape(-1, width)
    digits = pieces[:, rows : rows + 4, :rows].astype(jnp.int32)
    labels = digits[:, 0] | (digits[:, 1] << 8) | (digits[:, 2] << 16) | (digits[:, 3] << 24)
    return data, labels.reshape(-1)


def with_loss(grad_part, loss_part):
    count, rows, width = grad_part.shape
    tail = jnp.zeros((count, 8, width), grad_part.dtype).at[:, 0, :rows].set(loss_part)
    return jnp.concatenate([grad_part, tail], axis=1)


def pairings(digits):
    count = math.prod(size for size, _, _ in digits)
    steps = []
    for size, stride, ring in digits:
        bit = 1
        while bit < size:
            top = bit * 2 == size
            def partner(i, size=size, stride=stride, bit=bit, mirror=ring and top and size > 2):
                d = (i // stride) % size
                e = size - 1 - d if mirror else d ^ bit
                return i + (e - d) * stride
            steps.append([(i, partner(i)) for i in range(count)])
            bit *= 2
    return steps


def total_sums(sums, axes):
    for axis, digits in axes:
        for perm in pairings(digits):
            sums = sums + lax.ppermute(sums, axis, perm)
    return sums


def device_terms(informal, formal, labels, temp, bias):
    rows, width = informal.shape
    ngroup = lax.axis_size("group")
    nrow = lax.axis_size("bz")
    ncol = lax.axis_size("bx")
    root = math.sqrt(width)
    scale = temp / root
    row_informal, row_labels = split_labels(gather_by_shift(with_labels(informal, labels), "bz"), rows)
    col_formal, col_labels = split_labels(gather_by_shift(with_labels(formal, labels), "bx"), rows)
    raw = lax.dot_general(row_informal, col_formal, (((1,), (1,)), ((), ())), preferred_element_type=jnp.float32) / root
    logits = temp * raw + bias
    sign = jnp.where(row_labels[:, None] == col_labels[None, :], 1.0, -1.0).astype(jnp.float32)
    loss_part = jnp.sum(jax.nn.softplus(-sign * logits), axis=1)
    slope = -sign * jax.nn.sigmoid(-sign * logits)
    weights = slope.astype(jnp.bfloat16)
    grad_x_part = jnp.dot(weights, col_formal, preferred_element_type=jnp.float32)
    grad_y_part = lax.dot_general(weights, row_informal, (((0,), (0,)), ((), ())), preferred_element_type=jnp.float32)
    packed = reduce_by_shift(with_loss(grad_x_part.reshape(nrow, rows, width), loss_part.reshape(nrow, rows)), "bz")
    loss_sum = packed[rows, :rows]
    grad_x = scale * packed[:rows]
    grad_y = scale * reduce_by_shift(grad_y_part.reshape(ncol, rows, width), "bx")
    sums = total_sums(jnp.stack([jnp.sum(slope * raw), jnp.sum(slope)]), AXIS_DIGITS)
    set_size = rows * nrow * ncol
    total = jnp.float32(set_size * ngroup) * jnp.float32(set_size)
    loss = loss_sum / set_size
    return (loss, grad_x, grad_y, sums[0] / total, sums[1] / total)


AXIS_DIGITS = ()


def group_digits(mesh):
    column = mesh.devices[:, 0]
    ncore = len({d.core_on_chip for d in column})
    ny = len({d.coords[1] for d in column})
    nzh = column.size // (ny * ncore)
    if ny * nzh * ncore != column.size:
        return ((column.size, 1, False),)
    return ((ny, nzh * ncore, True), (nzh, ncore, True), (ncore, 1, False))


def split_blk(mesh):
    blk = mesh.devices[0]
    nx = len({d.coords[0] for d in blk})
    global AXIS_DIGITS
    AXIS_DIGITS = (
        ("group", group_digits(mesh)),
        ("bx", ((nx, 1, True),)),
        ("bz", ((blk.size // nx, 1, False),)),
    )
    grid = mesh.devices.reshape(mesh.shape["group"], nx, blk.size // nx)
    return Mesh(grid, ("group", "bx", "bz"))


def solution(mesh):
    fine = split_blk(mesh)
    rowspec = ("group", "bx", "bz")
    in_specs = (P(rowspec, None), P(rowspec, None), P(rowspec), P(), P())
    out_specs = (P(rowspec), P(rowspec, None), P(rowspec, None), P(), P())
    return jax.shard_map(device_terms, mesh=fine, in_specs=in_specs, out_specs=out_specs, check_vma=False)
```

```python
import math

import jax
import jax.numpy as jnp
from jax import lax
from jax.sharding import Mesh
from jax.sharding import PartitionSpec as P


def shifted(value, axis, by):
    count = lax.axis_size(axis)
    return lax.ppermute(value, axis, [(i, (i + by) % count) for i in range(count)])


def gather_by_shift(value, axis):
    count = lax.axis_size(axis)
    return jnp.concatenate([value] + [shifted(value, axis, k) for k in range(1, count)], axis=0)


def reduce_by_shift(parts, axis):
    count = lax.axis_size(axis)
    total = parts[0]
    for k in range(1, count):
        total = total + shifted(parts[k], axis, -k)
    return total


def with_labels(block, labels):
    rows, width = block.shape
    assert rows <= width
    shifts = 8 * jnp.arange(4, dtype=jnp.int32)
    digits = (labels[None, :] >> shifts[:, None]) & 255
    tail = jnp.zeros((16, width), block.dtype).at[:4, :rows].set(digits.astype(block.dtype))
    return jnp.concatenate([block, tail], axis=0)


def split_labels(gathered, rows):
    width = gathered.shape[1]
    pieces = gathered.reshape(-1, rows + 16, width)
    data = pieces[:, :rows].reshape(-1, width)
    digits = pieces[:, rows : rows + 4, :rows].astype(jnp.int32)
    labels = digits[:, 0] | (digits[:, 1] << 8) | (digits[:, 2] << 16) | (digits[:, 3] << 24)
    return data, labels.reshape(-1)


def with_loss(grad_part, loss_part):
    count, rows, width = grad_part.shape
    tail = jnp.zeros((count, 8, width), grad_part.dtype).at[:, 0, :rows].set(loss_part)
    return jnp.concatenate([grad_part, tail], axis=1)


def pairings(digits, count):
    steps = []
    for size, stride, ring in digits:
        bit = 1
        while bit < size:
            top = bit * 2 == size
            def partner(i, size=size, stride=stride, bit=bit, mirror=ring and top and size > 2):
                d = (i // stride) % size
                e = size - 1 - d if mirror else d ^ bit
                return i + (e - d) * stride
            steps.append([(i, partner(i)) for i in range(count)])
            bit *= 2
    return steps


def total_sums(sums, axes):
    for axis, digits in axes:
        for perm in pairings(digits, lax.axis_size(axis)):
            sums = sums + lax.ppermute(sums, axis, perm)
    return sums


def device_terms(informal, formal, labels, temp, bias):
    rows, width = informal.shape
    ngroup = lax.axis_size("group")
    nrow = lax.axis_size("bz")
    ncol = lax.axis_size("bx")
    root = math.sqrt(width)
    scale = temp / root
    row_informal, row_labels = split_labels(gather_by_shift(with_labels(informal, labels), "bz"), rows)
    col_formal, col_labels = split_labels(gather_by_shift(with_labels(formal, labels), "bx"), rows)
    raw = lax.dot_general(row_informal, col_formal, (((1,), (1,)), ((), ())), preferred_element_type=jnp.float32) / root
    logits = temp * raw + bias
    sign = jnp.where(row_labels[:, None] == col_labels[None, :], 1.0, -1.0).astype(jnp.float32)
    loss_part = jnp.sum(jax.nn.softplus(-sign * logits), axis=1)
    slope = -sign * jax.nn.sigmoid(-sign * logits)
    weights = slope.astype(jnp.bfloat16)
    grad_x_part = jnp.dot(weights, col_formal, preferred_element_type=jnp.float32)
    grad_y_part = lax.dot_general(weights, row_informal, (((0,), (0,)), ((), ())), preferred_element_type=jnp.float32)
    packed = reduce_by_shift(with_loss(grad_x_part.reshape(nrow, rows, width), loss_part.reshape(nrow, rows)), "bz")
    loss_sum = packed[rows, :rows]
    grad_x = scale * packed[:rows]
    grad_y = scale * reduce_by_shift(grad_y_part.reshape(ncol, rows, width), "bx")
    sums = total_sums(jnp.stack([jnp.sum(slope * raw), jnp.sum(slope)]), AXIS_DIGITS)
    set_size = rows * nrow * ncol
    total = jnp.float32(set_size * ngroup) * jnp.float32(set_size)
    loss = loss_sum / set_size
    return (loss, grad_x, grad_y, sums[0] / total, sums[1] / total)


AXIS_DIGITS = ()


def group_digits(mesh):
    column = mesh.devices[:, 0]
    ncore = len({d.core_on_chip for d in column})
    ny = len({d.coords[1] for d in column})
    nzh = column.size // (ny * ncore)
    if ny * nzh * ncore != column.size:
        return ((column.size, 1, False),), ()
    return ((ncore, 1, False), (ny, nzh * ncore, True)), ((nzh, ncore, True),)


def split_blk(mesh):
    blk = mesh.devices[0]
    nx = len({d.coords[0] for d in blk})
    global AXIS_DIGITS
    early, late = group_digits(mesh)
    AXIS_DIGITS = (
        ("group", early),
        ("bx", ((nx, 1, True),)),
        ("group", late),
        ("bz", ((blk.size // nx, 1, False),)),
    )
    grid = mesh.devices.reshape(mesh.shape["group"], nx, blk.size // nx)
    return Mesh(grid, ("group", "bx", "bz"))


def solution(mesh):
    fine = split_blk(mesh)
    rowspec = ("group", "bx", "bz")
    in_specs = (P(rowspec, None), P(rowspec, None), P(rowspec), P(), P())
    out_specs = (P(rowspec), P(rowspec, None), P(rowspec, None), P(), P())
    return jax.shard_map(device_terms, mesh=fine, in_specs=in_specs, out_specs=out_specs, check_vma=False)
```
